128 devices in a mesh: rep: 4 (over x), shard: 32 (over z, y, core).
Axes of the slice: x: 4, y: 4, z: 4, core: 2. Of those that a mesh axis runs over, the one named last changes fastest.
Arguments:
- features: bfloat16 [65536, 1024], P(('rep', 'shard')), may hold values from -6 to 6
- cotangent: bfloat16 [65536, 1024], P(('rep', 'shard')), may hold values from -6 to 6
- cross_weight: bfloat16 [1024, 1024], replicated, may hold values from -0.1875 to 0.1875
- cross_bias: float32 [1024], replicated, may hold values from -3 to 3
- emb_table: float32 [131072, 128], P('shard'), may hold values from -6 to 6
- row_accum: float32 [131072], P('shard'), may hold values from 0.5 to 50
- send_bags: int32 [128, 32, 256], P(('rep', 'shard')), may hold values from 0 to 3583, as said below
- slot_counts: int32 [128, 32], P(('rep', 'shard')), may hold values from 64 to 256, as said below
- recv_rows: int32 [128, 32, 256], P(('rep', 'shard')), may hold values from 0 to 4095, as said below
- touched_rows: int32 [32, 2048], P('shard'), may hold values from 0 to 4095, as said below
Outputs:
- weight_grad: float32 [1024, 1024], replicated
- bias_grad: float32 [1024], replicated
- dense_grad: bfloat16 [65536, 128], P(('rep', 'shard'))
- new_table: float32 [131072, 128], P('shard')
- new_accum: float32 [131072], P('shard')
The draws below stay inside these ranges and needn't reach their ends.
Inputs may be any that keep to these rules, and one draw needn't show every extreme that they name: `send_bags`: bag b * 7 + f of a device is feature f of its sample b. The first slot_counts[d, s] slots of a block are live; in each replica group some shard receives 256 live slots from every device of the group. `recv_rows`: every slot, live or not, names a row listed in touched_rows for the owner's shard. `touched_rows`: ascending and distinct.
All inputs are finite; a program needn't handle non-finite values.
Results may differ from the reference program's by a relative error of at most 0.0055.
Values may be sent and summed in bfloat16 or wider, within the bound.
No kernel may reach another device: no remote copies, remote signals or barrier semaphores. Data moves between devices by JAX's collectives and lax.ppermute only.
A program may use at most 128 MiB of HBM per device.

```python
import math
import jax
import jax.numpy as jnp
from jax import lax

E = 128
FEATS = 7
D = 1024
TOK_DEV = 512
TOKENS = 65536
SLOTS = 256
ROWS_DEV = 4096
TOUCHED = 2048
N_REP = 4
N_SHARD = 32


def plan_slots(key):
    base = jax.random.fold_in(key, 11)
    keys = jax.random.split(base, 5)
    quarter = SLOTS // 4
    picks = jax.vmap(lambda k: jax.random.permutation(k, ROWS_DEV - 2)[:TOUCHED - 2] + 1)(jax.random.split(keys[0], N_SHARD))
    ends = jnp.broadcast_to(jnp.array([0, ROWS_DEV - 1], jnp.int32), (N_SHARD, 2))
    touched = jnp.sort(jnp.concatenate([ends, picks.astype(jnp.int32)], axis=1), axis=1)
    hot = jax.random.randint(keys[1], (N_REP, 1, 1), 0, N_SHARD).astype(jnp.int32)
    counts = jax.random.randint(keys[2], (N_REP, N_SHARD, N_SHARD), quarter, 3 * quarter + 1).astype(jnp.int32)
    dest = jnp.arange(N_SHARD, dtype=jnp.int32)[None, None, :]
    counts = jnp.where(dest == hot, SLOTS, counts).astype(jnp.int32)
    place = jax.random.randint(keys[3], (N_REP, N_SHARD, N_SHARD, SLOTS), 0, TOUCHED).astype(jnp.int32)
    group = jnp.arange(N_REP, dtype=jnp.int32)[:, None, None, None]
    source = jnp.arange(N_SHARD, dtype=jnp.int32)[None, :, None, None]
    slot = jnp.arange(SLOTS, dtype=jnp.int32)[None, None, None, :]
    cover = source * quarter + slot
    place = jnp.where((group == 0) & (slot < quarter), cover, place).astype(jnp.int32)
    dest_full = jnp.broadcast_to(jnp.arange(N_SHARD, dtype=jnp.int32)[None, None, :, None], place.shape)
    rows = touched[dest_full, place]
    bags = jax.random.randint(keys[4], (N_REP, N_SHARD, N_SHARD, SLOTS), 0, TOK_DEV * FEATS).astype(jnp.int32)
    bags = bags.at[0, 0, 0, 0].set(TOK_DEV * FEATS - 1).at[0, 0, 0, 1].set(0)
    devices = N_REP * N_SHARD
    return (bags.reshape(devices, N_SHARD, SLOTS), counts.reshape(devices, N_SHARD), rows.transpose(0, 2, 1, 3).reshape(devices, N_SHARD, SLOTS), touched)


def draw_send_bags(key, part):
    return plan_slots(key)[0]


def draw_slot_counts(key, part):
    return plan_slots(key)[1]


def draw_recv_rows(key, part):
    return plan_slots(key)[2]


def draw_touched_rows(key, part):
    return plan_slots(key)[3]


def levels(own_key, extent, cuts, smallest, top_value):
    gain, own = 1.0, jax.random.fold_in(own_key, 6)
    for position, shards_of in cuts:
        heights = jnp.exp(jax.random.uniform(jax.random.fold_in(own, position), (shards_of,), jnp.float32, smallest / len(cuts), top_value / len(cuts)))
        gain = gain * jnp.repeat(heights, extent[position] // shards_of).reshape([-1 if axis == position else 1 for axis in range(len(extent))])
    return gain


def noise(own_key, extent, width, limit, cuts=(), held_as=jnp.bfloat16):
    result = width * jax.random.normal(own_key, extent, jnp.float32)
    if cuts:
        result = result * levels(own_key, extent, cuts, -0.22, 0.18)
    return jnp.clip(result, -limit, limit).astype(held_as)


def setup_inputs(seed: int = 0) -> dict:
    seeds = jax.random.split(jax.random.key(seed), 11)
    features = noise(seeds[0], (TOKENS, D), 1.0, 6.0, ((0, 128),))
    cotangent = noise(seeds[1], (TOKENS, D), 1.0, 6.0, ((0, 128),))
    cross_weight = noise(seeds[2], (D, D), D ** -0.5, 0.1875)
    cross_bias = noise(seeds[3], (D,), 0.5, 3.0, (), jnp.float32)
    emb_table = noise(seeds[4], (N_SHARD * ROWS_DEV, E), 1.0, 6.0, ((0, 32),), jnp.float32)
    row_accum = jnp.clip(jnp.exp(math.log(50.0) - 4.6051702 * jax.random.uniform(seeds[5], (N_SHARD * ROWS_DEV,), jnp.float32) ** levels(seeds[5], (N_SHARD * ROWS_DEV,), ((0, 32),), -0.2, 0.2)), 0.5, 50.0)
    send_bags = draw_send_bags(jax.random.fold_in(seeds[10], 71), 0)
    slot_counts = draw_slot_counts(jax.random.fold_in(seeds[10], 71), 0)
    recv_rows = draw_recv_rows(jax.random.fold_in(seeds[10], 71), 0)
    touched_rows = draw_touched_rows(jax.random.fold_in(seeds[10], 71), 0)
    return {"features": features, "cotangent": cotangent, "cross_weight": cross_weight, "cross_bias": cross_bias, "emb_table": emb_table, "row_accum": row_accum, "send_bags": send_bags, "slot_counts": slot_counts, "recv_rows": recv_rows, "touched_rows": touched_rows}


learn_rate = 0.5
keep_rate = 0.9

def adagrad_rows(table_rows, accum_rows, grads):
    new_accum = accum_rows + lax.optimization_barrier(jnp.mean(grads * grads, axis=1))
    new_rows = keep_rate * table_rows - learn_rate * grads / jnp.sqrt(new_accum)[:, None]
    return (new_rows, new_accum)

def reference(features, cotangent, cross_weight, cross_bias, emb_table, row_accum, send_bags, slot_counts, recv_rows, touched_rows):
    scale = 1.0 / jnp.sqrt(jnp.float32(TOKENS))
    linear = jnp.dot(features, cross_weight, preferred_element_type=jnp.float32) + cross_bias
    cot_f = cotangent.astype(jnp.float32)
    gated = (cot_f * features.astype(jnp.float32)).astype(jnp.bfloat16)
    weight_grad = jnp.dot(features.T, gated, preferred_element_type=jnp.float32) * scale
    bias_grad = lax.optimization_barrier(jnp.sum(gated.astype(jnp.float32), axis=0)) * scale
    backprop = jnp.dot(gated, cross_weight.T, preferred_element_type=jnp.float32)
    input_grad = cot_f * linear + backprop + cot_f
    dense_grad = input_grad[:, :E].astype(jnp.bfloat16)
    pooled = input_grad[:, E:].astype(jnp.bfloat16).reshape(TOKENS * FEATS, E)
    devices = N_REP * N_SHARD
    offsets = (jnp.arange(devices, dtype=jnp.int32) * (TOK_DEV * FEATS))[:, None, None]
    slot_grad = pooled[(send_bags + offsets).reshape(-1)].reshape(devices, N_SHARD, SLOTS, E)
    live_mask = jnp.arange(SLOTS, dtype=jnp.int32)[None, None, :] < slot_counts[:, :, None]
    slot_grad = jnp.where(live_mask[..., None], slot_grad, jnp.zeros((), jnp.bfloat16))
    arranged = slot_grad.reshape(N_REP, N_SHARD, N_SHARD, SLOTS, E).transpose(0, 2, 1, 3, 4)
    owners = jnp.arange(N_SHARD, dtype=jnp.int32)[None, :, None, None] * ROWS_DEV
    seg_ids = (recv_rows.reshape(N_REP, N_SHARD, N_SHARD, SLOTS) + owners).reshape(-1)
    row_grad = jax.ops.segment_sum(arranged.reshape(-1, E).astype(jnp.float32), seg_ids, num_segments=N_SHARD * ROWS_DEV)
    listed = (touched_rows + jnp.arange(N_SHARD, dtype=jnp.int32)[:, None] * ROWS_DEV).reshape(-1)
    marks = jnp.zeros((N_SHARD * ROWS_DEV,), jnp.int32).at[listed].set(1) > 0
    upd_table, upd_accum = adagrad_rows(emb_table, row_accum, row_grad)
    new_table = jnp.where(marks[:, None], upd_table, emb_table)
    new_accum = jnp.where(marks, upd_accum, row_accum)
    return (weight_grad, bias_grad, dense_grad, new_table, new_accum)
```

```python
import jax
import jax.numpy as jnp
from jax import lax
from jax.sharding import PartitionSpec as P

learn_rate = 0.5
keep_rate = 0.9


def adagrad_rows(table_rows, accum_rows, grads):
    new_accum = accum_rows + jnp.mean(grads * grads, axis=1)
    new_rows = keep_rate * table_rows - learn_rate * grads / jnp.sqrt(new_accum)[:, None]
    return (new_rows, new_accum)


def rep_sum(local, rep):
    rows = local.shape[0]
    parts = local.astype(jnp.bfloat16).reshape(rep, rows // rep, -1)
    got = lax.all_to_all(parts, "rep", 0, 0, tiled=True)
    mine = jnp.sum(got.astype(jnp.float32), axis=0).astype(jnp.bfloat16)
    spread = jnp.broadcast_to(mine[None], parts.shape)
    full = lax.all_to_all(spread, "rep", 0, 0, tiled=True)
    return full.reshape(rows, -1).astype(jnp.float32)


def per_device(
    features,
    cotangent,
    cross_weight,
    cross_bias,
    emb_table,
    row_accum,
    send_bags,
    slot_counts,
    recv_rows,
    touched_rows,
):
    width = emb_table.shape[1]
    shard_rows = emb_table.shape[0]
    dim = features.shape[1]
    rep = lax.axis_size("rep")
    total_tokens = features.shape[0] * rep * lax.axis_size("shard")
    scale = 1.0 / jnp.sqrt(jnp.float32(total_tokens))
    linear = jnp.dot(features, cross_weight, preferred_element_type=jnp.float32) + cross_bias
    cot_f = cotangent.astype(jnp.float32)
    gated = (cot_f * features.astype(jnp.float32)).astype(jnp.bfloat16)
    ones = jnp.ones((features.shape[0], 8), jnp.bfloat16)
    feats_aug = jnp.concatenate([features, ones], axis=1)
    grads_part = lax.dot_general(
        feats_aug, gated, (((0,), (0,)), ((), ())), preferred_element_type=jnp.float32
    )
    backprop = lax.dot_general(
        gated, cross_weight, (((1,), (1,)), ((), ())), preferred_element_type=jnp.float32
    )
    input_grad = cot_f * linear + backprop + cot_f
    dense_grad = input_grad[:, :width].astype(jnp.bfloat16)
    pooled = input_grad[:, width:].astype(jnp.bfloat16).reshape(-1, width)
    bag_ids = send_bags[0]
    shard_count = bag_ids.shape[0]
    slot_total = bag_ids.shape[1]
    live_mask = jnp.arange(slot_total, dtype=jnp.int32)[None, :] < slot_counts[0][:, None]
    picked = pooled.at[bag_ids.reshape(-1)].get(mode="promise_in_bounds")
    picked = picked.reshape(shard_count, slot_total, width)
    outgoing = jnp.where(live_mask[:, :, None], picked, jnp.zeros((), jnp.bfloat16))
    incoming = lax.all_to_all(outgoing, "shard", split_axis=0, concat_axis=0, tiled=True)
    grads_sum = lax.psum(grads_part, ("rep", "shard"))
    weight_grad = grads_sum[:dim] * scale
    bias_grad = grads_sum[dim] * scale
    incoming_rows = incoming.reshape(-1, width)
    slot_rows = recv_rows[0].reshape(-1)
    touched = touched_rows[0]
    row_range = jnp.arange(shard_rows, dtype=jnp.int32)
    marks = jnp.any(row_range[:, None] == touched[None, :], axis=1)
    select = (row_range[:, None] == slot_rows[None, :]).astype(jnp.bfloat16)
    local_sums = jnp.dot(select, incoming_rows, preferred_element_type=jnp.float32)
    row_grads = rep_sum(local_sums, rep)
    upd_table, upd_accum = adagrad_rows(emb_table, row_accum, row_grads)
    new_table = jnp.where(marks[:, None], upd_table, emb_table)
    new_accum = jnp.where(marks, upd_accum, row_accum)
    return (weight_grad, bias_grad, dense_grad, new_table, new_accum)


def solution(mesh):
    in_specs = (
        P(("rep", "shard"), None),
        P(("rep", "shard"), None),
        P(),
        P(),
        P("shard", None),
        P("shard"),
        P(("rep", "shard"), None, None),
        P(("rep", "shard"), None),
        P(("rep", "shard"), None, None),
        P("shard", None),
    )
    out_specs = (P(), P(), P(("rep", "shard"), None), P("shard", None), P("shard"))
    return jax.shard_map(
        per_device, mesh=mesh, in_specs=in_specs, out_specs=out_specs, check_vma=False
    )
```

```python
import jax
import jax.numpy as jnp
from jax import lax
from jax.sharding import PartitionSpec as P

learn_rate = 0.5
keep_rate = 0.9


def adagrad_rows(table_rows, accum_rows, grads):
    new_accum = accum_rows + jnp.mean(grads * grads, axis=1)
    new_rows = keep_rate * table_rows - learn_rate * grads / jnp.sqrt(new_accum)[:, None]
    return (new_rows, new_accum)


def rep_sum(local, rep):
    rows = local.shape[0]
    parts = local.astype(jnp.bfloat16).reshape(rep, rows // rep, -1)
    got = lax.all_to_all(parts, "rep", 0, 0, tiled=True)
    mine = jnp.sum(got.astype(jnp.float32), axis=0).astype(jnp.bfloat16)
    spread = jnp.broadcast_to(mine[None], parts.shape)
    full = lax.all_to_all(spread, "rep", 0, 0, tiled=True)
    return full.reshape(rows, -1).astype(jnp.float32)


def pack_grads(weight_part, bias_part, devices):
    dim = weight_part.shape[0]
    block = dim // devices
    bias_cols = jnp.pad(bias_part.reshape(devices, block, 1), ((0, 0), (0, 0), (0, 127)))
    packed = jnp.concatenate([weight_part.reshape(devices, block, dim), bias_cols], axis=2)
    return packed.astype(jnp.bfloat16)


def per_device(
    features,
    cotangent,
    cross_weight,
    cross_bias,
    emb_table,
    row_accum,
    send_bags,
    slot_counts,
    recv_rows,
    touched_rows,
):
    axes = ("rep", "shard")
    width = emb_table.shape[1]
    shard_rows = emb_table.shape[0]
    dim = features.shape[1]
    rep = lax.axis_size("rep")
    devices = lax.axis_size(axes)
    total_tokens = features.shape[0] * devices
    scale = 1.0 / jnp.sqrt(jnp.float32(total_tokens))
    linear = jnp.dot(features, cross_weight, preferred_element_type=jnp.float32) + cross_bias
    cot_f = cotangent.astype(jnp.float32)
    gated = (cot_f * features.astype(jnp.float32)).astype(jnp.bfloat16)
    weight_part = lax.dot_general(
        features, gated, (((0,), (0,)), ((), ())), preferred_element_type=jnp.float32
    )
    bias_part = jnp.sum(gated.astype(jnp.float32), axis=0)
    packed = pack_grads(weight_part, bias_part, devices)
    got_w = lax.all_to_all(packed, axes, 0, 0, tiled=True)

    backprop = lax.dot_general(
        gated, cross_weight, (((1,), (1,)), ((), ())), preferred_element_type=jnp.float32
    )
    input_grad = cot_f * linear + backprop + cot_f
    dense_grad = input_grad[:, :width].astype(jnp.bfloat16)
    pooled = input_grad[:, width:].astype(jnp.bfloat16).reshape(-1, width)
    bag_ids = send_bags[0]
    shard_count = bag_ids.shape[0]
    slot_total = bag_ids.shape[1]
    live_mask = jnp.arange(slot_total, dtype=jnp.int32)[None, :] < slot_counts[0][:, None]
    picked = pooled.at[bag_ids.reshape(-1)].get(mode="promise_in_bounds")
    picked = picked.reshape(shard_count, slot_total, width)
    outgoing = jnp.where(live_mask[:, :, None], picked, jnp.zeros((), jnp.bfloat16))

    got_w, outgoing = lax.optimization_barrier((got_w, outgoing))
    incoming = lax.all_to_all(outgoing, "shard", split_axis=0, concat_axis=0, tiled=True)
    ones = jnp.ones((devices,), jnp.bfloat16)
    mine_w = lax.dot_general(
        ones, got_w, (((0,), (0,)), ((), ())), preferred_element_type=jnp.float32
    ).astype(jnp.bfloat16)
    spread = jnp.broadcast_to(mine_w[None], got_w.shape)
    spread, incoming = lax.optimization_barrier((spread, incoming))
    full_w = lax.all_to_all(spread, axes, 0, 0, tiled=True)

    incoming_rows = incoming.reshape(-1, width)
    slot_rows = recv_rows[0].reshape(-1)
    touched = touched_rows[0]
    row_range = jnp.arange(shard_rows, dtype=jnp.int32)
    marks = jnp.any(row_range[:, None] == touched[None, :], axis=1)
    select = (row_range[:, None] == slot_rows[None, :]).astype(jnp.bfloat16)
    local_sums = jnp.dot(select, incoming_rows, preferred_element_type=jnp.float32)
    full_w, local_sums = lax.optimization_barrier((full_w, local_sums))
    row_grads = rep_sum(local_sums, rep)

    full_w = full_w.astype(jnp.float32)
    weight_grad = full_w[:, :, :dim].reshape(dim, dim) * scale
    bias_grad = full_w[:, :, dim].reshape(dim) * scale
    upd_table, upd_accum = adagrad_rows(emb_table, row_accum, row_grads)
    new_table = jnp.where(marks[:, None], upd_table, emb_table)
    new_accum = jnp.where(marks, upd_accum, row_accum)
    return (weight_grad, bias_grad, dense_grad, new_table, new_accum)


def solution(mesh):
    in_specs = (
        P(("rep", "shard"), None),
        P(("rep", "shard"), None),
        P(),
        P(),
        P("shard", None),
        P("shard"),
        P(("rep", "shard"), None, None),
        P(("rep", "shard"), None),
        P(("rep", "shard"), None, None),
        P("shard", None),
    )
    out_specs = (P(), P(), P(("rep", "shard"), None), P("shard", None), P("shard"))
    return jax.shard_map(
        per_device, mesh=mesh, in_specs=in_specs, out_specs=out_specs, check_vma=False
    )
```

```python
import jax
import jax.numpy as jnp
from jax import lax
from jax.sharding import PartitionSpec as P

learn_rate = 0.5
keep_rate = 0.9


def adagrad_rows(table_rows, accum_rows, grads):
    new_accum = accum_rows + jnp.mean(grads * grads, axis=1)
    new_rows = keep_rate * table_rows - learn_rate * grads / jnp.sqrt(new_accum)[:, None]
    return (new_rows, new_accum)


def rep_sum(local, rep):
    rows = local.shape[0]
    parts = local.astype(jnp.bfloat16).reshape(rep, rows // rep, -1)
    got = lax.all_to_all(parts, "rep", 0, 0, tiled=True)
    mine = jnp.sum(got.astype(jnp.float32), axis=0).astype(jnp.bfloat16)
    spread = jnp.broadcast_to(mine[None], parts.shape)
    full = lax.all_to_all(spread, "rep", 0, 0, tiled=True)
    return full.reshape(rows, -1).astype(jnp.float32)


def pack_grads(weight_part, bias_part, devices):
    dim = weight_part.shape[0]
    block = dim // devices
    bias_cols = jnp.pad(bias_part.reshape(devices, block, 1), ((0, 0), (0, 0), (0, 127)))
    packed = jnp.concatenate([weight_part.reshape(devices, block, dim), bias_cols], axis=2)
    return packed.astype(jnp.bfloat16)


def per_device(
    features,
    cotangent,
    cross_weight,
    cross_bias,
    emb_table,
    row_accum,
    send_bags,
    slot_counts,
    recv_rows,
    touched_rows,
):
    axes = ("rep", "shard")
    width = emb_table.shape[1]
    shard_rows = emb_table.shape[0]
    dim = features.shape[1]
    rep = lax.axis_size("rep")
    devices = lax.axis_size(axes)
    total_tokens = features.shape[0] * devices
    scale = 1.0 / jnp.sqrt(jnp.float32(total_tokens))
    linear = jnp.dot(features, cross_weight, preferred_element_type=jnp.float32) + cross_bias
    cot_f = cotangent.astype(jnp.float32)
    gated = (cot_f * features.astype(jnp.float32)).astype(jnp.bfloat16)
    weight_part = lax.dot_general(
        features, gated, (((0,), (0,)), ((), ())), preferred_element_type=jnp.float32
    )
    bias_part = jnp.sum(gated.astype(jnp.float32), axis=0)
    packed = pack_grads(weight_part, bias_part, devices)
    got_w = lax.all_to_all(packed, axes, 0, 0, tiled=True)

    backprop = lax.dot_general(
        gated, cross_weight, (((1,), (1,)), ((), ())), preferred_element_type=jnp.float32
    )
    input_grad = cot_f * linear + backprop + cot_f
    dense_grad = input_grad[:, :width].astype(jnp.bfloat16)
    pooled = input_grad[:, width:].astype(jnp.bfloat16).reshape(-1, width)
    bag_ids = send_bags[0]
    shard_count = bag_ids.shape[0]
    slot_total = bag_ids.shape[1]
    live_mask = jnp.arange(slot_total, dtype=jnp.int32)[None, :] < slot_counts[0][:, None]
    flat_bags = jnp.where(live_mask, bag_ids, -1).reshape(-1)
    bag_range = jnp.arange(pooled.shape[0], dtype=jnp.int32)
    pick = (flat_bags[:, None] == bag_range[None, :]).astype(jnp.bfloat16)
    picked = jnp.dot(pick, pooled, preferred_element_type=jnp.float32).astype(jnp.bfloat16)
    outgoing = picked.reshape(shard_count, slot_total, width)

    got_w, outgoing = lax.optimization_barrier((got_w, outgoing))
    incoming = lax.all_to_all(outgoing, "shard", split_axis=0, concat_axis=0, tiled=True)
    ones = jnp.ones((devices,), jnp.bfloat16)
    mine_w = lax.dot_general(
        ones, got_w, (((0,), (0,)), ((), ())), preferred_element_type=jnp.float32
    ).astype(jnp.bfloat16)
    spread = jnp.broadcast_to(mine_w[None], got_w.shape)
    spread, incoming = lax.optimization_barrier((spread, incoming))
    full_w = lax.all_to_all(spread, axes, 0, 0, tiled=True)

    incoming_rows = incoming.reshape(-1, width)
    slot_rows = recv_rows[0].reshape(-1)
    touched = touched_rows[0]
    select = (touched[:, None] == slot_rows[None, :]).astype(jnp.bfloat16)
    local_sums = jnp.dot(select, incoming_rows, preferred_element_type=jnp.float32)
    full_w, local_sums = lax.optimization_barrier((full_w, local_sums))
    touched_grads = rep_sum(local_sums, rep).astype(jnp.bfloat16)
    row_range = jnp.arange(shard_rows, dtype=jnp.int32)
    place = (row_range[:, None] == touched[None, :]).astype(jnp.bfloat16)
    with_marks = jnp.concatenate([touched_grads, jnp.ones_like(touched_grads)], axis=1)
    spread_rows = jnp.dot(place, with_marks, preferred_element_type=jnp.float32)
    row_grads = spread_rows[:, :width]
    marks = spread_rows[:, width] > 0.5

    full_w = full_w.astype(jnp.float32)
    weight_grad = full_w[:, :, :dim].reshape(dim, dim) * scale
    bias_grad = full_w[:, :, dim].reshape(dim) * scale
    upd_table, upd_accum = adagrad_rows(emb_table, row_accum, row_grads)
    new_table = jnp.where(marks[:, None], upd_table, emb_table)
    new_accum = jnp.where(marks, upd_accum, row_accum)
    return (weight_grad, bias_grad, dense_grad, new_table, new_accum)


def solution(mesh):
    in_specs = (
        P(("rep", "shard"), None),
        P(("rep", "shard"), None),
        P(),
        P(),
        P("shard", None),
        P("shard"),
        P(("rep", "shard"), None, None),
        P(("rep", "shard"), None),
        P(("rep", "shard"), None, None),
        P("shard", None),
    )
    out_specs = (P(), P(), P(("rep", "shard"), None), P("shard", None), P("shard"))
    return jax.shard_map(
        per_device, mesh=mesh, in_specs=in_specs, out_specs=out_specs, check_vma=False
    )
```

```python
import jax
import jax.numpy as jnp
from jax import lax
from jax.sharding import PartitionSpec as P

learn_rate = 0.5
keep_rate = 0.9


def adagrad_rows(table_rows, accum_rows, grads):
    new_accum = accum_rows + jnp.mean(grads * grads, axis=1)
    new_rows = keep_rate * table_rows - learn_rate * grads / jnp.sqrt(new_accum)[:, None]
    return (new_rows, new_accum)


def rep_sum(local, rep):
    rows = local.shape[0]
    parts = local.astype(jnp.bfloat16).reshape(rep, rows // rep, -1)
    got = lax.all_to_all(parts, "rep", 0, 0, tiled=True)
    mine = jnp.sum(got.astype(jnp.float32), axis=0).astype(jnp.bfloat16)
    spread = jnp.broadcast_to(mine[None], parts.shape)
    full = lax.all_to_all(spread, "rep", 0, 0, tiled=True)
    return full.reshape(rows, -1).astype(jnp.float32)


def pack_grads(weight_part, bias_part, devices):
    dim = weight_part.shape[0]
    block = dim // devices
    bias_cols = jnp.pad(bias_part.reshape(devices, block, 1), ((0, 0), (0, 0), (0, 127)))
    packed = jnp.concatenate([weight_part.reshape(devices, block, dim), bias_cols], axis=2)
    return packed.astype(jnp.bfloat16)


def per_device(
    features,
    cotangent,
    cross_weight,
    cross_bias,
    emb_table,
    row_accum,
    send_bags,
    slot_counts,
    recv_rows,
    touched_rows,
):
    axes = ("rep", "shard")
    width = emb_table.shape[1]
    shard_rows = emb_table.shape[0]
    dim = features.shape[1]
    rep = lax.axis_size("rep")
    devices = lax.axis_size(axes)
    total_tokens = features.shape[0] * devices
    scale = 1.0 / jnp.sqrt(jnp.float32(total_tokens))
    linear = jnp.dot(features, cross_weight, preferred_element_type=jnp.float32) + cross_bias
    cot_f = cotangent.astype(jnp.float32)
    gated = (cot_f * features.astype(jnp.float32)).astype(jnp.bfloat16)
    weight_part = lax.dot_general(
        features, gated, (((0,), (0,)), ((), ())), preferred_element_type=jnp.float32
    )
    bias_part = jnp.sum(gated.astype(jnp.float32), axis=0)
    packed = pack_grads(weight_part, bias_part, devices)
    got_w = lax.all_to_all(packed, axes, 0, 0, tiled=True)

    backprop = lax.dot_general(
        gated, cross_weight, (((1,), (1,)), ((), ())), preferred_element_type=jnp.float32
    )
    input_grad = cot_f * linear + backprop + cot_f
    dense_grad = input_grad[:, :width].astype(jnp.bfloat16)
    pooled = input_grad[:, width:].astype(jnp.bfloat16).reshape(-1, width)
    bag_ids = send_bags[0]
    shard_count = bag_ids.shape[0]
    slot_total = bag_ids.shape[1]
    live_mask = jnp.arange(slot_total, dtype=jnp.int32)[None, :] < slot_counts[0][:, None]
    flat_bags = jnp.where(live_mask, bag_ids, -1).reshape(-1)
    bag_range = jnp.arange(pooled.shape[0], dtype=jnp.int32)
    pick = (flat_bags[:, None] == bag_range[None, :]).astype(jnp.bfloat16)
    picked = jnp.dot(pick, pooled, preferred_element_type=jnp.float32).astype(jnp.bfloat16)
    outgoing = picked.reshape(shard_count, slot_total, width)

    got_w, outgoing = lax.optimization_barrier((got_w, outgoing))
    incoming = lax.all_to_all(outgoing, "shard", split_axis=0, concat_axis=0, tiled=True)
    ones = jnp.ones((devices,), jnp.bfloat16)
    mine_w = lax.dot_general(
        ones, got_w, (((0,), (0,)), ((), ())), preferred_element_type=jnp.float32
    ).astype(jnp.bfloat16)
    full_w = lax.all_gather(mine_w, axes, axis=0, tiled=False)

    incoming_rows = incoming.reshape(-1, width)
    slot_rows = recv_rows[0].reshape(-1)
    touched = touched_rows[0]
    select = (touched[:, None] == slot_rows[None, :]).astype(jnp.bfloat16)
    local_sums = jnp.dot(select, incoming_rows, preferred_element_type=jnp.float32)
    touched_grads = rep_sum(local_sums, rep).astype(jnp.bfloat16)
    row_range = jnp.arange(shard_rows, dtype=jnp.int32)
    place = (row_range[:, None] == touched[None, :]).astype(jnp.bfloat16)
    with_marks = jnp.concatenate([touched_grads, jnp.ones_like(touched_grads)], axis=1)
    spread_rows = jnp.dot(place, with_marks, preferred_element_type=jnp.float32)
    row_grads = spread_rows[:, :width]
    marks = spread_rows[:, width] > 0.5

    full_w = full_w.astype(jnp.float32).reshape(devices, -1, dim + 128)
    weight_grad = full_w[:, :, :dim].reshape(dim, dim) * scale
    bias_grad = full_w[:, :, dim].reshape(dim) * scale
    upd_table, upd_accum = adagrad_rows(emb_table, row_accum, row_grads)
    new_table = jnp.where(marks[:, None], upd_table, emb_table)
    new_accum = jnp.where(marks, upd_accum, row_accum)
    return (weight_grad, bias_grad, dense_grad, new_table, new_accum)


def solution(mesh):
    in_specs = (
        P(("rep", "shard"), None),
        P(("rep", "shard"), None),
        P(),
        P(),
        P("shard", None),
        P("shard"),
        P(("rep", "shard"), None, None),
        P(("rep", "shard"), None),
        P(("rep", "shard"), None, None),
        P("shard", None),
    )
    out_specs = (P(), P(), P(("rep", "shard"), None), P("shard", None), P("shard"))
    return jax.shard_map(
        per_device, mesh=mesh, in_specs=in_specs, out_specs=out_specs, check_vma=False
    )
```

```python
import jax
import jax.numpy as jnp
from jax import lax
from jax.sharding import PartitionSpec as P

learn_rate = 0.5
keep_rate = 0.9


def adagrad_rows(table_rows, accum_rows, grads):
    new_accum = accum_rows + jnp.mean(grads * grads, axis=1)
    new_rows = keep_rate * table_rows - learn_rate * grads / jnp.sqrt(new_accum)[:, None]
    return (new_rows, new_accum)


def rep_sum(local, rep):
    parts = jnp.broadcast_to(local.astype(jnp.bfloat16)[None], (rep,) + local.shape)
    got = lax.all_to_all(parts, "rep", 0, 0, tiled=True)
    total = got[0].astype(jnp.float32)
    for k in range(1, rep):
        total = total + got[k].astype(jnp.float32)
    return total


def pack_grads(weight_part, bias_part, devices):
    dim = weight_part.shape[0]
    block = dim // devices
    bias_cols = jnp.pad(bias_part.reshape(devices, block, 1), ((0, 0), (0, 0), (0, 127)))
    packed = jnp.concatenate([weight_part.reshape(devices, block, dim), bias_cols], axis=2)
    return packed.astype(jnp.bfloat16)


def per_device(
    features,
    cotangent,
    cross_weight,
    cross_bias,
    emb_table,
    row_accum,
    send_bags,
    slot_counts,
    recv_rows,
    touched_rows,
):
    axes = ("rep", "shard")
    width = emb_table.shape[1]
    shard_rows = emb_table.shape[0]
    dim = features.shape[1]
    rep = lax.axis_size("rep")
    devices = lax.axis_size(axes)
    total_tokens = features.shape[0] * devices
    scale = 1.0 / jnp.sqrt(jnp.float32(total_tokens))
    linear = jnp.dot(features, cross_weight, preferred_element_type=jnp.float32) + cross_bias
    cot_f = cotangent.astype(jnp.float32)
    gated = (cot_f * features.astype(jnp.float32)).astype(jnp.bfloat16)
    weight_part = lax.dot_general(
        features, gated, (((0,), (0,)), ((), ())), preferred_element_type=jnp.float32
    )
    bias_part = jnp.sum(gated.astype(jnp.float32), axis=0)
    packed = pack_grads(weight_part, bias_part, devices)
    got_w = lax.all_to_all(packed, axes, 0, 0, tiled=True)

    backprop = lax.dot_general(
        gated, cross_weight, (((1,), (1,)), ((), ())), preferred_element_type=jnp.float32
    )
    input_grad = cot_f * linear + backprop + cot_f
    dense_grad = input_grad[:, :width].astype(jnp.bfloat16)
    pooled = input_grad[:, width:].astype(jnp.bfloat16).reshape(-1, width)
    bag_ids = send_bags[0]
    shard_count = bag_ids.shape[0]
    slot_total = bag_ids.shape[1]
    live_mask = jnp.arange(slot_total, dtype=jnp.int32)[None, :] < slot_counts[0][:, None]
    flat_bags = jnp.where(live_mask, bag_ids, -1).reshape(-1)
    bag_range = jnp.arange(pooled.shape[0], dtype=jnp.int32)
    pick = (flat_bags[:, None] == bag_range[None, :]).astype(jnp.bfloat16)
    picked = jnp.dot(pick, pooled, preferred_element_type=jnp.float32).astype(jnp.bfloat16)
    outgoing = picked.reshape(shard_count, slot_total, width)

    got_w, outgoing = lax.optimization_barrier((got_w, outgoing))
    incoming = lax.all_to_all(outgoing, "shard", split_axis=0, concat_axis=0, tiled=True)
    ones = jnp.ones((devices,), jnp.bfloat16)
    mine_w = lax.dot_general(
        ones, got_w, (((0,), (0,)), ((), ())), preferred_element_type=jnp.float32
    ).astype(jnp.bfloat16)
    full_w = lax.all_gather(mine_w, axes, axis=0, tiled=False)

    incoming_rows = incoming.reshape(-1, width)
    slot_rows = recv_rows[0].reshape(-1)
    touched = touched_rows[0]
    select = (touched[:, None] == slot_rows[None, :]).astype(jnp.bfloat16)
    local_sums = jnp.dot(select, incoming_rows, preferred_element_type=jnp.float32)
    touched_grads = rep_sum(local_sums, rep).astype(jnp.bfloat16)
    row_range = jnp.arange(shard_rows, dtype=jnp.int32)
    place = (row_range[:, None] == touched[None, :]).astype(jnp.bfloat16)
    with_marks = jnp.concatenate([touched_grads, jnp.ones_like(touched_grads)], axis=1)
    spread_rows = jnp.dot(place, with_marks, preferred_element_type=jnp.float32)
    row_grads = spread_rows[:, :width]
    marks = spread_rows[:, width] > 0.5

    full_w = full_w.astype(jnp.float32).reshape(devices, -1, dim + 128)
    weight_grad = full_w[:, :, :dim].reshape(dim, dim) * scale
    bias_grad = full_w[:, :, dim].reshape(dim) * scale
    upd_table, upd_accum = adagrad_rows(emb_table, row_accum, row_grads)
    new_table = jnp.where(marks[:, None], upd_table, emb_table)
    new_accum = jnp.where(marks, upd_accum, row_accum)
    return (weight_grad, bias_grad, dense_grad, new_table, new_accum)


def solution(mesh):
    in_specs = (
        P(("rep", "shard"), None),
        P(("rep", "shard"), None),
        P(),
        P(),
        P("shard", None),
        P("shard"),
        P(("rep", "shard"), None, None),
        P(("rep", "shard"), None),
        P(("rep", "shard"), None, None),
        P("shard", None),
    )
    out_specs = (P(), P(), P(("rep", "shard"), None), P("shard", None), P("shard"))
    return jax.shard_map(
        per_device, mesh=mesh, in_specs=in_specs, out_specs=out_specs, check_vma=False
    )
```

```python
import functools

import jax
import jax.numpy as jnp
from jax import lax
from jax.experimental import pallas as pl
from jax.sharding import PartitionSpec as P

learn_rate = 0.5
keep_rate = 0.9


def adagrad_rows(table_rows, accum_rows, grads):
    new_accum = accum_rows + jnp.mean(grads * grads, axis=1)
    new_rows = keep_rate * table_rows - learn_rate * grads / jnp.sqrt(new_accum)[:, None]
    return (new_rows, new_accum)


def rep_sum(local, rep):
    rows = local.shape[0]
    parts = local.astype(jnp.bfloat16).reshape(rep, rows // rep, -1)
    got = lax.all_to_all(parts, "rep", 0, 0, tiled=True)
    mine = jnp.sum(got.astype(jnp.float32), axis=0).astype(jnp.bfloat16)
    spread = jnp.broadcast_to(mine[None], parts.shape)
    full = lax.all_to_all(spread, "rep", 0, 0, tiled=True)
    return full.reshape(rows, -1).astype(jnp.float32)


def pick_kernel(feats, t_ref, f_ref, p_ref, o_ref):
    tile = t_ref.shape[0]
    samples = p_ref.shape[0]
    width = o_ref.shape[1]
    sample_ids = lax.broadcasted_iota(jnp.int32, (tile, samples), 1)
    onehot = (t_ref[...] == sample_ids).astype(jnp.bfloat16)
    f_ids = f_ref[...]
    acc = jnp.zeros((tile, width), jnp.float32)
    for f in range(feats):
        block = p_ref[:, f * width:(f + 1) * width]
        part = jnp.dot(onehot, block, preferred_element_type=jnp.float32)
        acc = jnp.where(f_ids == f, part, acc)
    o_ref[...] = acc.astype(o_ref.dtype)


def pick_rows(pooled_cols, t_ids, f_ids, feats, tile=512):
    samples, cols = pooled_cols.shape
    width = cols // feats
    slots = t_ids.shape[0]
    cost = pl.CostEstimate(
        flops=2 * slots * samples * cols,
        transcendentals=0,
        bytes_accessed=samples * cols * 2 + slots * 8 + slots * width * 2,
    )
    return pl.pallas_call(
        functools.partial(pick_kernel, feats),
        grid=(slots // tile,),
        in_specs=[
            pl.BlockSpec((tile, 1), lambda i: (i, 0)),
            pl.BlockSpec((tile, 1), lambda i: (i, 0)),
            pl.BlockSpec((samples, cols), lambda i: (0, 0)),
        ],
        out_specs=pl.BlockSpec((tile, width), lambda i: (i, 0)),
        out_shape=jax.ShapeDtypeStruct((slots, width), jnp.bfloat16),
        cost_estimate=cost,
    )(t_ids, f_ids, pooled_cols)


def pack_grads(weight_part, bias_part, devices):
    dim = weight_part.shape[0]
    block = dim // devices
    bias_cols = jnp.pad(bias_part.reshape(devices, block, 1), ((0, 0), (0, 0), (0, 127)))
    packed = jnp.concatenate([weight_part.reshape(devices, block, dim), bias_cols], axis=2)
    return packed.astype(jnp.bfloat16)


def per_device(
    features,
    cotangent,
    cross_weight,
    cross_bias,
    emb_table,
    row_accum,
    send_bags,
    slot_counts,
    recv_rows,
    touched_rows,
):
    axes = ("rep", "shard")
    width = emb_table.shape[1]
    shard_rows = emb_table.shape[0]
    dim = features.shape[1]
    rep = lax.axis_size("rep")
    devices = lax.axis_size(axes)
    total_tokens = features.shape[0] * devices
    scale = 1.0 / jnp.sqrt(jnp.float32(total_tokens))
    linear = jnp.dot(features, cross_weight, preferred_element_type=jnp.float32) + cross_bias
    cot_f = cotangent.astype(jnp.float32)
    gated = (cot_f * features.astype(jnp.float32)).astype(jnp.bfloat16)
    weight_part = lax.dot_general(
        features, gated, (((0,), (0,)), ((), ())), preferred_element_type=jnp.float32
    )
    bias_part = jnp.sum(gated.astype(jnp.float32), axis=0)
    packed = pack_grads(weight_part, bias_part, devices)
    got_w = lax.all_to_all(packed, axes, 0, 0, tiled=True)

    backprop = lax.dot_general(
        gated, cross_weight, (((1,), (1,)), ((), ())), preferred_element_type=jnp.float32
    )
    input_grad = cot_f * linear + backprop + cot_f
    dense_grad = input_grad[:, :width].astype(jnp.bfloat16)
    pooled_cols = input_grad[:, width:].astype(jnp.bfloat16)
    feats = pooled_cols.shape[1] // width
    bag_ids = send_bags[0]
    shard_count = bag_ids.shape[0]
    slot_total = bag_ids.shape[1]
    live_mask = jnp.arange(slot_total, dtype=jnp.int32)[None, :] < slot_counts[0][:, None]
    t_ids = jnp.where(live_mask, bag_ids // feats, -1).reshape(-1, 1)
    f_ids = (bag_ids % feats).reshape(-1, 1)
    picked = pick_rows(pooled_cols, t_ids, f_ids, feats)
    outgoing = picked.reshape(shard_count, slot_total, width)

    got_w, outgoing = lax.optimization_barrier((got_w, outgoing))
    incoming = lax.all_to_all(outgoing, "shard", split_axis=0, concat_axis=0, tiled=True)
    ones = jnp.ones((devices,), jnp.bfloat16)
    mine_w = lax.dot_general(
        ones, got_w, (((0,), (0,)), ((), ())), preferred_element_type=jnp.float32
    ).astype(jnp.bfloat16)
    full_w = lax.all_gather(mine_w, axes, axis=0, tiled=False)

    incoming_rows = incoming.reshape(-1, width)
    slot_rows = recv_rows[0].reshape(-1)
    touched = touched_rows[0]
    select = (touched[:, None] == slot_rows[None, :]).astype(jnp.bfloat16)
    local_sums = jnp.dot(select, incoming_rows, preferred_element_type=jnp.float32)
    touched_grads = rep_sum(local_sums, rep).astype(jnp.bfloat16)
    row_range = jnp.arange(shard_rows, dtype=jnp.int32)
    place = (row_range[:, None] == touched[None, :]).astype(jnp.bfloat16)
    with_marks = jnp.concatenate([touched_grads, jnp.ones_like(touched_grads)], axis=1)
    spread_rows = jnp.dot(place, with_marks, preferred_element_type=jnp.float32)
    row_grads = spread_rows[:, :width]
    marks = spread_rows[:, width] > 0.5

    full_w = full_w.astype(jnp.float32).reshape(devices, -1, dim + 128)
    weight_grad = full_w[:, :, :dim].reshape(dim, dim) * scale
    bias_grad = full_w[:, :, dim].reshape(dim) * scale
    upd_table, upd_accum = adagrad_rows(emb_table, row_accum, row_grads)
    new_table = jnp.where(marks[:, None], upd_table, emb_table)
    new_accum = jnp.where(marks, upd_accum, row_accum)
    return (weight_grad, bias_grad, dense_grad, new_table, new_accum)


def solution(mesh):
    in_specs = (
        P(("rep", "shard"), None),
        P(("rep", "shard"), None),
        P(),
        P(),
        P("shard", None),
        P("shard"),
        P(("rep", "shard"), None, None),
        P(("rep", "shard"), None),
        P(("rep", "shard"), None, None),
        P("shard", None),
    )
    out_specs = (P(), P(), P(("rep", "shard"), None), P("shard", None), P("shard"))
    return jax.shard_map(
        per_device, mesh=mesh, in_specs=in_specs, out_specs=out_specs, check_vma=False
    )
```

```python
import jax
import jax.numpy as jnp
from jax import lax
from jax.sharding import PartitionSpec as P

learn_rate = 0.5
keep_rate = 0.9


def adagrad_rows(table_rows, accum_rows, grads):
    new_accum = accum_rows + jnp.mean(grads * grads, axis=1)
    new_rows = keep_rate * table_rows - learn_rate * grads / jnp.sqrt(new_accum)[:, None]
    return (new_rows, new_accum)


def rep_sum(local, rep):
    rows = local.shape[0]
    parts = local.astype(jnp.bfloat16).reshape(rep, rows // rep, -1)
    got = lax.all_to_all(parts, "rep", 0, 0, tiled=True)
    mine = jnp.sum(got.astype(jnp.float32), axis=0).astype(jnp.bfloat16)
    spread = jnp.broadcast_to(mine[None], parts.shape)
    full = lax.all_to_all(spread, "rep", 0, 0, tiled=True)
    return full.reshape(rows, -1).astype(jnp.float32)


def pack_grads(weight_part, bias_part, devices):
    dim = weight_part.shape[0]
    block = dim // devices
    bias_cols = jnp.pad(bias_part.reshape(devices, block, 1), ((0, 0), (0, 0), (0, 127)))
    packed = jnp.concatenate([weight_part.reshape(devices, block, dim), bias_cols], axis=2)
    return packed.astype(jnp.bfloat16)


def per_device(
    features,
    cotangent,
    cross_weight,
    cross_bias,
    emb_table,
    row_accum,
    send_bags,
    slot_counts,
    recv_rows,
    touched_rows,
):
    axes = ("rep", "shard")
    width = emb_table.shape[1]
    shard_rows = emb_table.shape[0]
    dim = features.shape[1]
    rep = lax.axis_size("rep")
    devices = lax.axis_size(axes)
    total_tokens = features.shape[0] * devices
    scale = 1.0 / jnp.sqrt(jnp.float32(total_tokens))
    linear = jnp.dot(features, cross_weight, preferred_element_type=jnp.float32) + cross_bias
    cot_f = cotangent.astype(jnp.float32)
    gated = (cot_f * features.astype(jnp.float32)).astype(jnp.bfloat16)
    weight_part = lax.dot_general(
        features, gated, (((0,), (0,)), ((), ())), preferred_element_type=jnp.float32
    )
    bias_part = jnp.sum(gated.astype(jnp.float32), axis=0)
    packed = pack_grads(weight_part, bias_part, devices)
    got_w = lax.all_to_all(packed, axes, 0, 0, tiled=True)

    backprop = lax.dot_general(
        gated, cross_weight, (((1,), (1,)), ((), ())), preferred_element_type=jnp.float32
    )
    input_grad = cot_f * linear + backprop + cot_f
    dense_grad = input_grad[:, :width].astype(jnp.bfloat16)
    pooled = input_grad[:, width:].astype(jnp.bfloat16).reshape(-1, width)
    bag_ids = send_bags[0]
    shard_count = bag_ids.shape[0]
    slot_total = bag_ids.shape[1]
    live_mask = jnp.arange(slot_total, dtype=jnp.int32)[None, :] < slot_counts[0][:, None]
    flat_bags = jnp.where(live_mask, bag_ids, -1).reshape(-1)
    bag_range = jnp.arange(pooled.shape[0], dtype=jnp.int32)
    pick = (flat_bags[:, None] == bag_range[None, :]).astype(jnp.bfloat16)
    picked = jnp.dot(pick, pooled, preferred_element_type=jnp.float32).astype(jnp.bfloat16)
    outgoing = picked.reshape(shard_count, slot_total, width)

    got_w, outgoing = lax.optimization_barrier((got_w, outgoing))
    incoming = lax.all_to_all(outgoing, "shard", split_axis=0, concat_axis=0, tiled=True)
    ones = jnp.ones((devices,), jnp.bfloat16)
    mine_w = lax.dot_general(
        ones, got_w, (((0,), (0,)), ((), ())), preferred_element_type=jnp.float32
    ).astype(jnp.bfloat16)
    full_w = lax.all_gather(mine_w, axes, axis=0, tiled=True)

    incoming_rows = incoming.reshape(-1, width)
    slot_rows = recv_rows[0].reshape(-1)
    touched = touched_rows[0]
    select = (touched[:, None] == slot_rows[None, :]).astype(jnp.bfloat16)
    local_sums = jnp.dot(select, incoming_rows, preferred_element_type=jnp.float32)
    touched_grads = rep_sum(local_sums, rep).astype(jnp.bfloat16)
    row_range = jnp.arange(shard_rows, dtype=jnp.int32)
    place = (row_range[:, None] == touched[None, :]).astype(jnp.bfloat16)
    with_marks = jnp.concatenate([touched_grads, jnp.ones_like(touched_grads)], axis=1)
    spread_rows = jnp.dot(place, with_marks, preferred_element_type=jnp.float32)
    row_grads = spread_rows[:, :width]
    marks = spread_rows[:, width] > 0.5

    weight_grad = full_w[:, :dim].astype(jnp.float32) * scale
    bias_grad = full_w[:, dim].astype(jnp.float32) * scale
    upd_table, upd_accum = adagrad_rows(emb_table, row_accum, row_grads)
    new_table = jnp.where(marks[:, None], upd_table, emb_table)
    new_accum = jnp.where(marks, upd_accum, row_accum)
    return (weight_grad, bias_grad, dense_grad, new_table, new_accum)


def solution(mesh):
    in_specs = (
        P(("rep", "shard"), None),
        P(("rep", "shard"), None),
        P(),
        P(),
        P("shard", None),
        P("shard"),
        P(("rep", "shard"), None, None),
        P(("rep", "shard"), None),
        P(("rep", "shard"), None, None),
        P("shard", None),
    )
    out_specs = (P(), P(), P(("rep", "shard"), None), P("shard", None), P("shard"))
    return jax.shard_map(
        per_device, mesh=mesh, in_specs=in_specs, out_specs=out_specs, check_vma=False
    )
```

```python
import jax
import jax.numpy as jnp
from jax import lax
from jax.sharding import PartitionSpec as P

learn_rate = 0.5
keep_rate = 0.9


def adagrad_rows(table_rows, accum_rows, grads):
    new_accum = accum_rows + jnp.mean(grads * grads, axis=1)
    new_rows = keep_rate * table_rows - learn_rate * grads / jnp.sqrt(new_accum)[:, None]
    return (new_rows, new_accum)


def rep_sum(local, rep):
    rows = local.shape[0]
    parts = local.astype(jnp.bfloat16).reshape(rep, rows // rep, -1)
    got = lax.all_to_all(parts, "rep", 0, 0, tiled=True)
    mine = jnp.sum(got.astype(jnp.float32), axis=0).astype(jnp.bfloat16)
    spread = jnp.broadcast_to(mine[None], parts.shape)
    full = lax.all_to_all(spread, "rep", 0, 0, tiled=True)
    return full.reshape(rows, -1).astype(jnp.float32)


def per_device(
    features,
    cotangent,
    cross_weight,
    cross_bias,
    emb_table,
    row_accum,
    send_bags,
    slot_counts,
    recv_rows,
    touched_rows,
):
    axes = ("rep", "shard")
    width = emb_table.shape[1]
    shard_rows = emb_table.shape[0]
    dim = features.shape[1]
    rep = lax.axis_size("rep")
    devices = lax.axis_size(axes)
    total_tokens = features.shape[0] * devices
    scale = 1.0 / jnp.sqrt(jnp.float32(total_tokens))
    linear = jnp.dot(features, cross_weight, preferred_element_type=jnp.float32) + cross_bias
    cot_f = cotangent.astype(jnp.float32)
    gated = (cot_f * features.astype(jnp.float32)).astype(jnp.bfloat16)
    lanes = 128
    feats_ones = jnp.concatenate(
        [features, jnp.ones((features.shape[0], lanes), jnp.bfloat16)], axis=1
    )
    terms_t = lax.dot_general(
        gated, feats_ones, (((0,), (0,)), ((), ())), preferred_element_type=jnp.float32
    )
    packed = terms_t.astype(jnp.bfloat16).reshape(devices, dim // devices, dim + lanes)
    got_w = lax.all_to_all(packed, axes, 0, 0, tiled=True)

    backprop = lax.dot_general(
        gated, cross_weight, (((1,), (1,)), ((), ())), preferred_element_type=jnp.float32
    )
    input_grad = cot_f * linear + backprop + cot_f
    dense_grad = input_grad[:, :width].astype(jnp.bfloat16)
    pooled = input_grad[:, width:].astype(jnp.bfloat16).reshape(-1, width)
    bag_ids = send_bags[0]
    shard_count = bag_ids.shape[0]
    slot_total = bag_ids.shape[1]
    live_mask = jnp.arange(slot_total, dtype=jnp.int32)[None, :] < slot_counts[0][:, None]
    flat_bags = jnp.where(live_mask, bag_ids, -1).reshape(-1)
    bag_range = jnp.arange(pooled.shape[0], dtype=jnp.int32)
    pick = (flat_bags[:, None] == bag_range[None, :]).astype(jnp.bfloat16)
    picked = jnp.dot(pick, pooled, preferred_element_type=jnp.float32).astype(jnp.bfloat16)
    outgoing = picked.reshape(shard_count, slot_total, width)

    got_w, outgoing = lax.optimization_barrier((got_w, outgoing))
    incoming = lax.all_to_all(outgoing, "shard", split_axis=0, concat_axis=0, tiled=True)
    ones = jnp.ones((devices,), jnp.bfloat16)
    mine_w = lax.dot_general(
        ones, got_w, (((0,), (0,)), ((), ())), preferred_element_type=jnp.float32
    ).astype(jnp.bfloat16)
    full_w = lax.all_gather(mine_w, axes, axis=0, tiled=True)

    row_range = jnp.arange(shard_rows, dtype=jnp.int32)
    place = (row_range[:, None] == touched_rows[0][None, :]).astype(jnp.bfloat16)
    place, incoming = lax.optimization_barrier((place, incoming))
    incoming_rows = incoming.reshape(-1, width)
    slot_rows = recv_rows[0].reshape(-1)
    touched = touched_rows[0]
    select = (touched[:, None] == slot_rows[None, :]).astype(jnp.bfloat16)
    local_sums = jnp.dot(select, incoming_rows, preferred_element_type=jnp.float32)
    touched_grads = rep_sum(local_sums, rep).astype(jnp.bfloat16)
    with_marks = jnp.concatenate([touched_grads, jnp.ones_like(touched_grads)], axis=1)
    spread_rows = jnp.dot(place, with_marks, preferred_element_type=jnp.float32)
    row_grads = spread_rows[:, :width]
    marks = spread_rows[:, width] > 0.5

    weight_grad = full_w[:, :dim].T.astype(jnp.float32) * scale
    bias_grad = full_w[:, dim].astype(jnp.float32) * scale
    upd_table, upd_accum = adagrad_rows(emb_table, row_accum, row_grads)
    new_table = jnp.where(marks[:, None], upd_table, emb_table)
    new_accum = jnp.where(marks, upd_accum, row_accum)
    return (weight_grad, bias_grad, dense_grad, new_table, new_accum)


def solution(mesh):
    in_specs = (
        P(("rep", "shard"), None),
        P(("rep", "shard"), None),
        P(),
        P(),
        P("shard", None),
        P("shard"),
        P(("rep", "shard"), None, None),
        P(("rep", "shard"), None),
        P(("rep", "shard"), None, None),
        P("shard", None),
    )
    out_specs = (P(), P(), P(("rep", "shard"), None), P("shard", None), P("shard"))
    return jax.shard_map(
        per_device, mesh=mesh, in_specs=in_specs, out_specs=out_specs, check_vma=False
    )
```

```python
import jax
import jax.numpy as jnp
from jax import lax
from jax.sharding import PartitionSpec as P

learn_rate = 0.5
keep_rate = 0.9


def adagrad_rows(table_rows, accum_rows, grads):
    new_accum = accum_rows + jnp.mean(grads * grads, axis=1)
    new_rows = keep_rate * table_rows - learn_rate * grads / jnp.sqrt(new_accum)[:, None]
    return (new_rows, new_accum)


def rep_sum(local, rep):
    rows = local.shape[0]
    parts = local.astype(jnp.bfloat16).reshape(rep, rows // rep, -1)
    got = lax.all_to_all(parts, "rep", 0, 0, tiled=True)
    mine = jnp.sum(got.astype(jnp.float32), axis=0).astype(jnp.bfloat16)
    spread = jnp.broadcast_to(mine[None], parts.shape)
    full = lax.all_to_all(spread, "rep", 0, 0, tiled=True)
    return full.reshape(rows, -1).astype(jnp.float32)


def per_device(
    features,
    cotangent,
    cross_weight,
    cross_bias,
    emb_table,
    row_accum,
    send_bags,
    slot_counts,
    recv_rows,
    touched_rows,
):
    axes = ("rep", "shard")
    width = emb_table.shape[1]
    shard_rows = emb_table.shape[0]
    dim = features.shape[1]
    rep = lax.axis_size("rep")
    devices = lax.axis_size(axes)
    total_tokens = features.shape[0] * devices
    scale = 1.0 / jnp.sqrt(jnp.float32(total_tokens))
    linear = jnp.dot(features, cross_weight, preferred_element_type=jnp.float32) + cross_bias
    cot_f = cotangent.astype(jnp.float32)
    gated = (cot_f * features.astype(jnp.float32)).astype(jnp.bfloat16)
    lanes = 128
    feats_ones = jnp.concatenate(
        [features, jnp.ones((features.shape[0], lanes), jnp.bfloat16)], axis=1
    )
    terms_t = lax.dot_general(
        gated, feats_ones, (((0,), (0,)), ((), ())), preferred_element_type=jnp.float32
    )
    packed = terms_t.astype(jnp.bfloat16).reshape(devices, dim // devices, dim + lanes)
    got_w = lax.all_to_all(packed, axes, 0, 0, tiled=True)

    backprop = lax.dot_general(
        gated, cross_weight, (((1,), (1,)), ((), ())), preferred_element_type=jnp.float32
    )
    input_grad = cot_f * linear + backprop + cot_f
    dense_grad = input_grad[:, :width].astype(jnp.bfloat16)
    pooled = input_grad[:, width:].astype(jnp.bfloat16).reshape(-1, width)
    bag_ids = send_bags[0]
    shard_count = bag_ids.shape[0]
    slot_total = bag_ids.shape[1]
    live_mask = jnp.arange(slot_total, dtype=jnp.int32)[None, :] < slot_counts[0][:, None]
    flat_bags = jnp.where(live_mask, bag_ids, -1).reshape(-1)
    bag_range = jnp.arange(pooled.shape[0], dtype=jnp.int32)
    pick = (flat_bags[:, None] == bag_range[None, :]).astype(jnp.bfloat16)
    picked = jnp.dot(pick, pooled, preferred_element_type=jnp.float32).astype(jnp.bfloat16)
    outgoing = picked.reshape(shard_count, slot_total, width)

    got_w, outgoing = lax.optimization_barrier((got_w, outgoing))
    incoming = lax.all_to_all(outgoing, "shard", split_axis=0, concat_axis=0, tiled=True)
    ones = jnp.ones((devices,), jnp.bfloat16)
    mine_w = lax.dot_general(
        ones, got_w, (((0,), (0,)), ((), ())), preferred_element_type=jnp.float32
    ).astype(jnp.bfloat16)
    full_w = lax.all_gather(mine_w, axes, axis=0, tiled=True)

    incoming_rows = incoming.reshape(-1, width)
    slot_rows = recv_rows[0].reshape(-1)
    touched = touched_rows[0]
    select = (touched[:, None] == slot_rows[None, :]).astype(jnp.bfloat16)
    local_sums = jnp.dot(select, incoming_rows, preferred_element_type=jnp.float32)
    touched_grads = rep_sum(local_sums, rep).astype(jnp.bfloat16)
    row_range = jnp.arange(shard_rows, dtype=jnp.int32)
    place = (row_range[:, None] == touched[None, :]).astype(jnp.bfloat16)
    with_marks = jnp.concatenate([touched_grads, jnp.ones_like(touched_grads)], axis=1)
    spread_rows = jnp.dot(place, with_marks, preferred_element_type=jnp.float32)
    row_grads = spread_rows[:, :width]
    marks = spread_rows[:, width] > 0.5

    eye = (lax.broadcasted_iota(jnp.int32, (dim, dim), 0) == lax.broadcasted_iota(jnp.int32, (dim, dim), 1)).astype(jnp.bfloat16)
    weight_t = lax.dot_general(
        full_w[:, :dim], eye, (((0,), (0,)), ((), ())), preferred_element_type=jnp.float32
    )
    weight_grad = weight_t * scale
    bias_grad = full_w[:, dim].astype(jnp.float32) * scale
    upd_table, upd_accum = adagrad_rows(emb_table, row_accum, row_grads)
    new_table = jnp.where(marks[:, None], upd_table, emb_table)
    new_accum = jnp.where(marks, upd_accum, row_accum)
    return (weight_grad, bias_grad, dense_grad, new_table, new_accum)


def solution(mesh):
    in_specs = (
        P(("rep", "shard"), None),
        P(("rep", "shard"), None),
        P(),
        P(),
        P("shard", None),
        P("shard"),
        P(("rep", "shard"), None, None),
        P(("rep", "shard"), None),
        P(("rep", "shard"), None, None),
        P("shard", None),
    )
    out_specs = (P(), P(), P(("rep", "shard"), None), P("shard", None), P("shard"))
    return jax.shard_map(
        per_device, mesh=mesh, in_specs=in_specs, out_specs=out_specs, check_vma=False
    )
```

```python
import jax
import jax.numpy as jnp
from jax import lax
from jax.sharding import PartitionSpec as P

learn_rate = 0.5
keep_rate = 0.9


def adagrad_rows(table_rows, accum_rows, grads):
    new_accum = accum_rows + jnp.mean(grads * grads, axis=1)
    new_rows = keep_rate * table_rows - learn_rate * grads / jnp.sqrt(new_accum)[:, None]
    return (new_rows, new_accum)


def rep_sum(local, rep):
    rows = local.shape[0]
    parts = local.astype(jnp.bfloat16).reshape(rep, rows // rep, -1)
    got = lax.all_to_all(parts, "rep", 0, 0, tiled=True)
    mine = jnp.sum(got.astype(jnp.float32), axis=0).astype(jnp.bfloat16)
    spread = jnp.broadcast_to(mine[None], parts.shape)
    full = lax.all_to_all(spread, "rep", 0, 0, tiled=True)
    return full.reshape(rows, -1).astype(jnp.float32)


def per_device(
    features,
    cotangent,
    cross_weight,
    cross_bias,
    emb_table,
    row_accum,
    send_bags,
    slot_counts,
    recv_rows,
    touched_rows,
):
    axes = ("rep", "shard")
    width = emb_table.shape[1]
    shard_rows = emb_table.shape[0]
    dim = features.shape[1]
    rep = lax.axis_size("rep")
    devices = lax.axis_size(axes)
    total_tokens = features.shape[0] * devices
    scale = 1.0 / jnp.sqrt(jnp.float32(total_tokens))
    linear = jnp.dot(features, cross_weight, preferred_element_type=jnp.float32) + cross_bias
    cot_f = cotangent.astype(jnp.float32)
    gated = (cot_f * features.astype(jnp.float32)).astype(jnp.bfloat16)
    lanes = 128
    feats_ones = jnp.concatenate(
        [features, jnp.ones((features.shape[0], lanes), jnp.bfloat16)], axis=1
    )
    terms_t = lax.dot_general(
        gated, feats_ones, (((0,), (0,)), ((), ())), preferred_element_type=jnp.float32
    )
    packed = terms_t.astype(jnp.bfloat16).reshape(devices, dim // devices, dim + lanes)
    got_w = lax.all_to_all(packed, axes, 0, 0, tiled=True)

    backprop = lax.dot_general(
        gated, cross_weight, (((1,), (1,)), ((), ())), preferred_element_type=jnp.float32
    )
    input_grad = cot_f * linear + backprop + cot_f
    dense_grad = input_grad[:, :width].astype(jnp.bfloat16)
    pooled = input_grad[:, width:].astype(jnp.bfloat16).reshape(-1, width)
    bag_ids = send_bags[0]
    shard_count = bag_ids.shape[0]
    slot_total = bag_ids.shape[1]
    live_mask = jnp.arange(slot_total, dtype=jnp.int32)[None, :] < slot_counts[0][:, None]
    flat_bags = jnp.where(live_mask, bag_ids, -1).reshape(-1)
    bag_range = jnp.arange(pooled.shape[0], dtype=jnp.int32)
    pick = (flat_bags[:, None] == bag_range[None, :]).astype(jnp.bfloat16)
    picked = jnp.dot(pick, pooled, preferred_element_type=jnp.float32).astype(jnp.bfloat16)
    outgoing = picked.reshape(shard_count, slot_total, width)

    got_w, outgoing = lax.optimization_barrier((got_w, outgoing))
    ones = jnp.ones((devices,), jnp.bfloat16)
    mine_w = lax.dot_general(
        ones, got_w, (((0,), (0,)), ((), ())), preferred_element_type=jnp.float32
    ).astype(jnp.bfloat16)
    mine_w, outgoing = lax.optimization_barrier((mine_w, outgoing))
    incoming = lax.all_to_all(outgoing, "shard", split_axis=0, concat_axis=0, tiled=True)
    full_w = lax.all_gather(mine_w, axes, axis=0, tiled=True)

    incoming_rows = incoming.reshape(-1, width)
    slot_rows = recv_rows[0].reshape(-1)
    touched = touched_rows[0]
    select = (touched[:, None] == slot_rows[None, :]).astype(jnp.bfloat16)
    local_sums = jnp.dot(select, incoming_rows, preferred_element_type=jnp.float32)
    touched_grads = rep_sum(local_sums, rep).astype(jnp.bfloat16)
    row_range = jnp.arange(shard_rows, dtype=jnp.int32)
    place = (row_range[:, None] == touched[None, :]).astype(jnp.bfloat16)
    with_marks = jnp.concatenate([touched_grads, jnp.ones_like(touched_grads)], axis=1)
    spread_rows = jnp.dot(place, with_marks, preferred_element_type=jnp.float32)
    row_grads = spread_rows[:, :width]
    marks = spread_rows[:, width] > 0.5

    eye = (lax.broadcasted_iota(jnp.int32, (dim, dim), 0) == lax.broadcasted_iota(jnp.int32, (dim, dim), 1)).astype(jnp.bfloat16)
    weight_t = lax.dot_general(
        full_w[:, :dim], eye, (((0,), (0,)), ((), ())), preferred_element_type=jnp.float32
    )
    weight_grad = weight_t * scale
    bias_grad = jnp.mean(full_w[:, dim:].astype(jnp.float32), axis=1) * scale
    upd_table, upd_accum = adagrad_rows(emb_table, row_accum, row_grads)
    new_table = jnp.where(marks[:, None], upd_table, emb_table)
    new_accum = jnp.where(marks, upd_accum, row_accum)
    return (weight_grad, bias_grad, dense_grad, new_table, new_accum)


def solution(mesh):
    in_specs = (
        P(("rep", "shard"), None),
        P(("rep", "shard"), None),
        P(),
        P(),
        P("shard", None),
        P("shard"),
        P(("rep", "shard"), None, None),
        P(("rep", "shard"), None),
        P(("rep", "shard"), None, None),
        P("shard", None),
    )
    out_specs = (P(), P(), P(("rep", "shard"), None), P("shard", None), P("shard"))
    return jax.shard_map(
        per_device, mesh=mesh, in_specs=in_specs, out_specs=out_specs, check_vma=False
    )
```

```python
import jax
import jax.numpy as jnp
from jax import lax
from jax.sharding import PartitionSpec as P

learn_rate = 0.5
keep_rate = 0.9


def adagrad_rows(table_rows, accum_rows, grads):
    new_accum = accum_rows + jnp.mean(grads * grads, axis=1)
    new_rows = keep_rate * table_rows - learn_rate * grads / jnp.sqrt(new_accum)[:, None]
    return (new_rows, new_accum)


def rep_sum(local, rep):
    rows = local.shape[0]
    parts = local.astype(jnp.bfloat16).reshape(rep, rows // rep, -1)
    got = lax.all_to_all(parts, "rep", 0, 0, tiled=True)
    mine = jnp.sum(got.astype(jnp.float32), axis=0).astype(jnp.bfloat16)
    spread = jnp.broadcast_to(mine[None], parts.shape)
    full = lax.all_to_all(spread, "rep", 0, 0, tiled=True)
    return full.reshape(rows, -1).astype(jnp.float32)


def per_device(
    features,
    cotangent,
    cross_weight,
    cross_bias,
    emb_table,
    row_accum,
    send_bags,
    slot_counts,
    recv_rows,
    touched_rows,
):
    axes = ("rep", "shard")
    width = emb_table.shape[1]
    shard_rows = emb_table.shape[0]
    dim = features.shape[1]
    rep = lax.axis_size("rep")
    devices = lax.axis_size(axes)
    total_tokens = features.shape[0] * devices
    scale = 1.0 / jnp.sqrt(jnp.float32(total_tokens))
    linear = jnp.dot(features, cross_weight, preferred_element_type=jnp.float32) + cross_bias
    cot_f = cotangent.astype(jnp.float32)
    gated = (cot_f * features.astype(jnp.float32)).astype(jnp.bfloat16)
    lanes = 128
    feats_ones = jnp.concatenate(
        [features, jnp.ones((features.shape[0], lanes), jnp.bfloat16)], axis=1
    )
    terms_t = lax.dot_general(
        gated, feats_ones, (((0,), (0,)), ((), ())), preferred_element_type=jnp.float32
    )
    packed = terms_t.astype(jnp.bfloat16).reshape(devices, dim // devices, dim + lanes)
    got_w = lax.all_to_all(packed, axes, 0, 0, tiled=True)

    backprop = lax.dot_general(
        gated, cross_weight, (((1,), (1,)), ((), ())), preferred_element_type=jnp.float32
    )
    input_grad = cot_f * linear + backprop + cot_f
    dense_grad = input_grad[:, :width].astype(jnp.bfloat16)
    pooled = input_grad[:, width:].astype(jnp.bfloat16).reshape(-1, width)
    bag_ids = send_bags[0]
    shard_count = bag_ids.shape[0]
    slot_total = bag_ids.shape[1]
    live_mask = jnp.arange(slot_total, dtype=jnp.int32)[None, :] < slot_counts[0][:, None]
    flat_bags = jnp.where(live_mask, bag_ids, -1).reshape(-1)
    bag_range = jnp.arange(pooled.shape[0], dtype=jnp.int32)
    pick = (flat_bags[:, None] == bag_range[None, :]).astype(jnp.bfloat16)
    picked = jnp.dot(pick, pooled, preferred_element_type=jnp.float32).astype(jnp.bfloat16)
    outgoing = picked.reshape(shard_count, slot_total, width)

    got_w, outgoing = lax.optimization_barrier((got_w, outgoing))
    half = slot_total // 2
    incoming_a = lax.all_to_all(outgoing[:, :half], "shard", 0, 0, tiled=True)
    incoming_b = lax.all_to_all(outgoing[:, half:], "shard", 0, 0, tiled=True)
    ones = jnp.ones((devices,), jnp.bfloat16)
    mine_w = lax.dot_general(
        ones, got_w, (((0,), (0,)), ((), ())), preferred_element_type=jnp.float32
    ).astype(jnp.bfloat16)
    full_w = lax.all_gather(mine_w, axes, axis=0, tiled=True)

    touched = touched_rows[0]

    def touched_sums(slots, rows):
        select = (touched[:, None] == rows.reshape(-1)[None, :]).astype(jnp.bfloat16)
        return jnp.dot(select, slots.reshape(-1, width), preferred_element_type=jnp.float32)

    local_sums = touched_sums(incoming_a, recv_rows[0][:, :half]) + touched_sums(
        incoming_b, recv_rows[0][:, half:]
    )
    touched_grads = rep_sum(local_sums, rep).astype(jnp.bfloat16)
    row_range = jnp.arange(shard_rows, dtype=jnp.int32)
    place = (row_range[:, None] == touched[None, :]).astype(jnp.bfloat16)
    with_marks = jnp.concatenate([touched_grads, jnp.ones_like(touched_grads)], axis=1)
    spread_rows = jnp.dot(place, with_marks, preferred_element_type=jnp.float32)
    row_grads = spread_rows[:, :width]
    marks = spread_rows[:, width] > 0.5

    eye = (lax.broadcasted_iota(jnp.int32, (dim, dim), 0) == lax.broadcasted_iota(jnp.int32, (dim, dim), 1)).astype(jnp.bfloat16)
    weight_t = lax.dot_general(
        full_w[:, :dim], eye, (((0,), (0,)), ((), ())), preferred_element_type=jnp.float32
    )
    weight_grad = weight_t * scale
    bias_grad = jnp.mean(full_w[:, dim:].astype(jnp.float32), axis=1) * scale
    upd_table, upd_accum = adagrad_rows(emb_table, row_accum, row_grads)
    new_table = jnp.where(marks[:, None], upd_table, emb_table)
    new_accum = jnp.where(marks, upd_accum, row_accum)
    return (weight_grad, bias_grad, dense_grad, new_table, new_accum)


def solution(mesh):
    in_specs = (
        P(("rep", "shard"), None),
        P(("rep", "shard"), None),
        P(),
        P(),
        P("shard", None),
        P("shard"),
        P(("rep", "shard"), None, None),
        P(("rep", "shard"), None),
        P(("rep", "shard"), None, None),
        P("shard", None),
    )
    out_specs = (P(), P(), P(("rep", "shard"), None), P("shard", None), P("shard"))
    return jax.shard_map(
        per_device, mesh=mesh, in_specs=in_specs, out_specs=out_specs, check_vma=False
    )
```

```python
import jax
import jax.numpy as jnp
from jax import lax
from jax.sharding import PartitionSpec as P

learn_rate = 0.5
keep_rate = 0.9


def adagrad_rows(table_rows, accum_rows, grads):
    new_accum = accum_rows + jnp.mean(grads * grads, axis=1)
    new_rows = keep_rate * table_rows - learn_rate * grads / jnp.sqrt(new_accum)[:, None]
    return (new_rows, new_accum)


def rep_sum(local, rep):
    rows = local.shape[0]
    parts = local.astype(jnp.bfloat16).reshape(rep, rows // rep, -1)
    got = lax.all_to_all(parts, "rep", 0, 0, tiled=True)
    mine = jnp.sum(got.astype(jnp.float32), axis=0).astype(jnp.bfloat16)
    spread = jnp.broadcast_to(mine[None], parts.shape)
    full = lax.all_to_all(spread, "rep", 0, 0, tiled=True)
    return full.reshape(rows, -1).astype(jnp.float32)


def per_device(
    features,
    cotangent,
    cross_weight,
    cross_bias,
    emb_table,
    row_accum,
    send_bags,
    slot_counts,
    recv_rows,
    touched_rows,
):
    axes = ("rep", "shard")
    width = emb_table.shape[1]
    shard_rows = emb_table.shape[0]
    dim = features.shape[1]
    rep = lax.axis_size("rep")
    devices = lax.axis_size(axes)
    total_tokens = features.shape[0] * devices
    scale = 1.0 / jnp.sqrt(jnp.float32(total_tokens))
    linear = jnp.dot(features, cross_weight, preferred_element_type=jnp.float32) + cross_bias
    cot_f = cotangent.astype(jnp.float32)
    gated = (cot_f * features.astype(jnp.float32)).astype(jnp.bfloat16)
    lanes = 128
    feats_ones = jnp.concatenate(
        [features, jnp.ones((features.shape[0], lanes), jnp.bfloat16)], axis=1
    )
    terms_t = lax.dot_general(
        gated, feats_ones, (((0,), (0,)), ((), ())), preferred_element_type=jnp.float32
    )
    packed = terms_t.astype(jnp.bfloat16).reshape(devices, dim // devices, dim + lanes)
    got_w = lax.all_to_all(packed, axes, 0, 0, tiled=True)

    backprop = lax.dot_general(
        gated, cross_weight, (((1,), (1,)), ((), ())), preferred_element_type=jnp.float32
    )
    input_grad = cot_f * linear + backprop + cot_f
    dense_grad = input_grad[:, :width].astype(jnp.bfloat16)
    pooled = input_grad[:, width:].astype(jnp.bfloat16).reshape(-1, width)
    bag_ids = send_bags[0]
    shard_count = bag_ids.shape[0]
    slot_total = bag_ids.shape[1]
    live_mask = jnp.arange(slot_total, dtype=jnp.int32)[None, :] < slot_counts[0][:, None]
    flat_bags = jnp.where(live_mask, bag_ids, -1).reshape(-1)
    bag_range = jnp.arange(pooled.shape[0], dtype=jnp.int32)
    pick = (flat_bags[:, None] == bag_range[None, :]).astype(jnp.bfloat16)
    picked = jnp.dot(pick, pooled, preferred_element_type=jnp.float32).astype(jnp.bfloat16)
    outgoing = picked.reshape(shard_count, slot_total, width)

    got_w, outgoing = lax.optimization_barrier((got_w, outgoing))
    incoming = lax.all_to_all(outgoing, "shard", split_axis=0, concat_axis=0, tiled=True)
    ones = jnp.ones((devices,), jnp.bfloat16)
    mine_w = lax.dot_general(
        ones, got_w, (((0,), (0,)), ((), ())), preferred_element_type=jnp.float32
    ).astype(jnp.bfloat16)
    full_w = lax.all_gather(mine_w, axes, axis=0, tiled=True)

    incoming_rows = incoming.reshape(-1, width)
    slot_rows = recv_rows[0].reshape(-1)
    touched = touched_rows[0]
    select = (touched[:, None] == slot_rows[None, :]).astype(jnp.bfloat16)
    local_sums = jnp.dot(select, incoming_rows, preferred_element_type=jnp.float32)
    touched_grads = rep_sum(local_sums, rep).astype(jnp.bfloat16)
    row_range = jnp.arange(shard_rows, dtype=jnp.int32)
    place = (row_range[:, None] == touched[None, :]).astype(jnp.bfloat16)
    with_marks = jnp.concatenate([touched_grads, jnp.ones_like(touched_grads)], axis=1)
    spread_rows = jnp.dot(place, with_marks, preferred_element_type=jnp.float32)
    row_grads = spread_rows[:, :width]
    marks = spread_rows[:, width] > 0.5

    eye = (lax.broadcasted_iota(jnp.int32, (dim, dim), 0) == lax.broadcasted_iota(jnp.int32, (dim, dim), 1)).astype(jnp.bfloat16)
    weight_t = lax.dot_general(
        full_w[:, :dim], eye, (((0,), (0,)), ((), ())), preferred_element_type=jnp.float32
    )
    weight_grad = weight_t * scale
    bias_grad = jnp.mean(full_w[:, dim:].astype(jnp.float32), axis=1) * scale
    upd_table, upd_accum = adagrad_rows(emb_table, row_accum, row_grads)
    new_table = jnp.where(marks[:, None], upd_table, emb_table)
    new_accum = jnp.where(marks, upd_accum, row_accum)
    return (weight_grad, bias_grad, dense_grad, new_table, new_accum)


def solution(mesh):
    in_specs = (
        P(("rep", "shard"), None),
        P(("rep", "shard"), None),
        P(),
        P(),
        P("shard", None),
        P("shard"),
        P(("rep", "shard"), None, None),
        P(("rep", "shard"), None),
        P(("rep", "shard"), None, None),
        P("shard", None),
    )
    out_specs = (P(), P(), P(("rep", "shard"), None), P("shard", None), P("shard"))
    return jax.shard_map(
        per_device, mesh=mesh, in_specs=in_specs, out_specs=out_specs, check_vma=False
    )
```

```python
import jax
import jax.numpy as jnp
from jax import lax
from jax.sharding import PartitionSpec as P

learn_rate = 0.5
keep_rate = 0.9


def adagrad_rows(table_rows, accum_rows, grads):
    new_accum = accum_rows + jnp.mean(grads * grads, axis=1)
    new_rows = keep_rate * table_rows - learn_rate * grads / jnp.sqrt(new_accum)[:, None]
    return (new_rows, new_accum)


def rep_sum(local, rep):
    rows = local.shape[0]
    parts = local.astype(jnp.bfloat16).reshape(rep, rows // rep, -1)
    got = lax.all_to_all(parts, "rep", 0, 0, tiled=True)
    mine = jnp.sum(got.astype(jnp.float32), axis=0).astype(jnp.bfloat16)
    spread = jnp.broadcast_to(mine[None], parts.shape)
    full = lax.all_to_all(spread, "rep", 0, 0, tiled=True)
    return full.reshape(rows, -1).astype(jnp.float32)


def per_device(
    features,
    cotangent,
    cross_weight,
    cross_bias,
    emb_table,
    row_accum,
    send_bags,
    slot_counts,
    recv_rows,
    touched_rows,
):
    axes = ("rep", "shard")
    width = emb_table.shape[1]
    shard_rows = emb_table.shape[0]
    dim = features.shape[1]
    rep = lax.axis_size("rep")
    devices = lax.axis_size(axes)
    total_tokens = features.shape[0] * devices
    scale = 1.0 / jnp.sqrt(jnp.float32(total_tokens))
    linear = jnp.dot(features, cross_weight, preferred_element_type=jnp.float32) + cross_bias
    cot_f = cotangent.astype(jnp.float32)
    gated = (cot_f * features.astype(jnp.float32)).astype(jnp.bfloat16)
    lanes = 128
    feats_ones = jnp.concatenate(
        [features, jnp.ones((features.shape[0], lanes), jnp.bfloat16)], axis=1
    )
    terms_t = lax.dot_general(
        gated, feats_ones, (((0,), (0,)), ((), ())), preferred_element_type=jnp.float32
    )
    packed = terms_t.astype(jnp.bfloat16).reshape(devices, dim // devices, dim + lanes)
    got_w = lax.all_to_all(packed, axes, 0, 0, tiled=True)

    backprop = lax.dot_general(
        gated, cross_weight, (((1,), (1,)), ((), ())), preferred_element_type=jnp.float32
    )
    input_grad = cot_f * linear + backprop + cot_f
    dense_grad = input_grad[:, :width].astype(jnp.bfloat16)
    pooled = input_grad[:, width:].astype(jnp.bfloat16).reshape(-1, width)
    bag_ids = send_bags[0]
    shard_count = bag_ids.shape[0]
    slot_total = bag_ids.shape[1]
    live_mask = jnp.arange(slot_total, dtype=jnp.int32)[None, :] < slot_counts[0][:, None]
    flat_bags = jnp.where(live_mask, bag_ids, -1).reshape(-1)
    bag_range = jnp.arange(pooled.shape[0], dtype=jnp.int32)
    pick = (flat_bags[:, None] == bag_range[None, :]).astype(jnp.bfloat16)
    picked = jnp.dot(pick, pooled, preferred_element_type=jnp.float32).astype(jnp.bfloat16)
    outgoing = picked.reshape(shard_count, slot_total, width)

    got_w, outgoing = lax.optimization_barrier((got_w, outgoing))
    incoming = lax.all_to_all(outgoing, "shard", split_axis=0, concat_axis=0, tiled=True)
    ones = jnp.ones((devices,), jnp.bfloat16)
    mine_w = lax.dot_general(
        ones, got_w, (((0,), (0,)), ((), ())), preferred_element_type=jnp.float32
    ).astype(jnp.bfloat16)
    full_w = lax.all_gather(mine_w, axes, axis=0, tiled=True)

    marks = jnp.zeros((shard_rows,), jnp.bool_).at[touched_rows[0]].set(True, unique_indices=True)
    marks, incoming = lax.optimization_barrier((marks, incoming))
    incoming_rows = incoming.reshape(-1, width)
    slot_rows = recv_rows[0].reshape(-1)
    touched = touched_rows[0]
    select = (touched[:, None] == slot_rows[None, :]).astype(jnp.bfloat16)
    local_sums = jnp.dot(select, incoming_rows, preferred_element_type=jnp.float32)
    touched_grads = rep_sum(local_sums, rep).astype(jnp.bfloat16)
    row_range = jnp.arange(shard_rows, dtype=jnp.int32)
    place = (row_range[:, None] == touched[None, :]).astype(jnp.bfloat16)
    row_grads = jnp.dot(place, touched_grads, preferred_element_type=jnp.float32)

    eye = (lax.broadcasted_iota(jnp.int32, (dim, dim), 0) == lax.broadcasted_iota(jnp.int32, (dim, dim), 1)).astype(jnp.bfloat16)
    weight_t = lax.dot_general(
        full_w[:, :dim], eye, (((0,), (0,)), ((), ())), preferred_element_type=jnp.float32
    )
    weight_grad = weight_t * scale
    bias_grad = jnp.mean(full_w[:, dim:].astype(jnp.float32), axis=1) * scale
    upd_table, upd_accum = adagrad_rows(emb_table, row_accum, row_grads)
    new_table = jnp.where(marks[:, None], upd_table, emb_table)
    new_accum = jnp.where(marks, upd_accum, row_accum)
    return (weight_grad, bias_grad, dense_grad, new_table, new_accum)


def solution(mesh):
    in_specs = (
        P(("rep", "shard"), None),
        P(("rep", "shard"), None),
        P(),
        P(),
        P("shard", None),
        P("shard"),
        P(("rep", "shard"), None, None),
        P(("rep", "shard"), None),
        P(("rep", "shard"), None, None),
        P("shard", None),
    )
    out_specs = (P(), P(), P(("rep", "shard"), None), P("shard", None), P("shard"))
    return jax.shard_map(
        per_device, mesh=mesh, in_specs=in_specs, out_specs=out_specs, check_vma=False
    )
```

```python
import jax
import jax.numpy as jnp
from jax import lax
from jax.sharding import PartitionSpec as P

learn_rate = 0.5
keep_rate = 0.9


def adagrad_rows(table_rows, accum_rows, grads):
    new_accum = accum_rows + jnp.mean(grads * grads, axis=1)
    new_rows = keep_rate * table_rows - learn_rate * grads / jnp.sqrt(new_accum)[:, None]
    return (new_rows, new_accum)


def rep_sum(local, rep):
    rows = local.shape[0]
    parts = local.astype(jnp.bfloat16).reshape(rep, rows // rep, -1)
    got = lax.all_to_all(parts, "rep", 0, 0, tiled=True)
    mine = jnp.sum(got.astype(jnp.float32), axis=0).astype(jnp.bfloat16)
    spread = jnp.broadcast_to(mine[None], parts.shape)
    full = lax.all_to_all(spread, "rep", 0, 0, tiled=True)
    return full.reshape(rows, -1).astype(jnp.float32)


def per_device(
    features,
    cotangent,
    cross_weight,
    cross_bias,
    emb_table,
    row_accum,
    send_bags,
    slot_counts,
    recv_rows,
    touched_rows,
):
    axes = ("rep", "shard")
    width = emb_table.shape[1]
    shard_rows = emb_table.shape[0]
    dim = features.shape[1]
    rep = lax.axis_size("rep")
    devices = lax.axis_size(axes)
    total_tokens = features.shape[0] * devices
    scale = 1.0 / jnp.sqrt(jnp.float32(total_tokens))
    linear = jnp.dot(features, cross_weight, preferred_element_type=jnp.float32) + cross_bias
    cot_f = cotangent.astype(jnp.float32)
    gated = (cot_f * features.astype(jnp.float32)).astype(jnp.bfloat16)
    lanes = 128
    feats_ones = jnp.concatenate(
        [features, jnp.ones((features.shape[0], lanes), jnp.bfloat16)], axis=1
    )
    terms_t = lax.dot_general(
        gated, feats_ones, (((0,), (0,)), ((), ())), preferred_element_type=jnp.float32
    )
    packed = terms_t.astype(jnp.bfloat16).reshape(devices, dim // devices, dim + lanes)
    got_w = lax.all_to_all(packed, axes, 0, 0, tiled=True)

    backprop = lax.dot_general(
        gated, cross_weight, (((1,), (1,)), ((), ())), preferred_element_type=jnp.float32
    )
    input_grad = cot_f * linear + backprop + cot_f
    dense_grad = input_grad[:, :width].astype(jnp.bfloat16)
    pooled = input_grad[:, width:].astype(jnp.bfloat16).reshape(-1, width)
    bag_ids = send_bags[0]
    shard_count = bag_ids.shape[0]
    slot_total = bag_ids.shape[1]
    live_mask = jnp.arange(slot_total, dtype=jnp.int32)[None, :] < slot_counts[0][:, None]
    flat_bags = jnp.where(live_mask, bag_ids, -1).reshape(-1)
    bag_range = jnp.arange(pooled.shape[0], dtype=jnp.int32)
    pick = (flat_bags[:, None] == bag_range[None, :]).astype(jnp.bfloat16)
    picked = jnp.dot(pick, pooled, preferred_element_type=jnp.float32).astype(jnp.bfloat16)
    outgoing = picked.reshape(shard_count, slot_total, width)

    got_w, outgoing = lax.optimization_barrier((got_w, outgoing))
    incoming = lax.all_to_all(outgoing, "shard", split_axis=0, concat_axis=0, tiled=True)
    ones = jnp.ones((devices,), jnp.bfloat16)
    mine_w = lax.dot_general(
        ones, got_w, (((0,), (0,)), ((), ())), preferred_element_type=jnp.float32
    ).astype(jnp.bfloat16)
    full_w = lax.all_gather(mine_w, axes, axis=0, tiled=True)

    incoming_rows = incoming.reshape(-1, width)
    slot_rows = recv_rows[0].reshape(-1)
    touched = touched_rows[0]
    select = (slot_rows[:, None] == touched[None, :]).astype(jnp.bfloat16)
    local_sums = lax.dot_general(
        select, incoming_rows, (((0,), (0,)), ((), ())), preferred_element_type=jnp.float32
    )
    touched_grads = rep_sum(local_sums, rep).astype(jnp.bfloat16)
    row_range = jnp.arange(shard_rows, dtype=jnp.int32)
    place = (row_range[:, None] == touched[None, :]).astype(jnp.bfloat16)
    with_marks = jnp.concatenate([touched_grads, jnp.ones_like(touched_grads)], axis=1)
    spread_rows = jnp.dot(place, with_marks, preferred_element_type=jnp.float32)
    row_grads = spread_rows[:, :width]
    marks = spread_rows[:, width] > 0.5

    eye = (lax.broadcasted_iota(jnp.int32, (dim, dim), 0) == lax.broadcasted_iota(jnp.int32, (dim, dim), 1)).astype(jnp.bfloat16)
    weight_t = lax.dot_general(
        full_w[:, :dim], eye, (((0,), (0,)), ((), ())), preferred_element_type=jnp.float32
    )
    weight_grad = weight_t * scale
    bias_grad = jnp.mean(full_w[:, dim:].astype(jnp.float32), axis=1) * scale
    upd_table, upd_accum = adagrad_rows(emb_table, row_accum, row_grads)
    new_table = jnp.where(marks[:, None], upd_table, emb_table)
    new_accum = jnp.where(marks, upd_accum, row_accum)
    return (weight_grad, bias_grad, dense_grad, new_table, new_accum)


def solution(mesh):
    in_specs = (
        P(("rep", "shard"), None),
        P(("rep", "shard"), None),
        P(),
        P(),
        P("shard", None),
        P("shard"),
        P(("rep", "shard"), None, None),
        P(("rep", "shard"), None),
        P(("rep", "shard"), None, None),
        P("shard", None),
    )
    out_specs = (P(), P(), P(("rep", "shard"), None), P("shard", None), P("shard"))
    return jax.shard_map(
        per_device, mesh=mesh, in_specs=in_specs, out_specs=out_specs, check_vma=False
    )
```
